256 devices in a mesh: tile: 16 (over z_lo, y), visit: 16 (over z_hi, x, core).
Axes of the slice: x: 4, y: 4, z: 8 (z_hi: 2, z_lo: 4; z = z_hi * 4 + z_lo), core: 2. Of those that a mesh axis runs over, the one named last changes fastest.
Arguments:
- template: float32 [2048, 2048], P('tile', 'visit'), may hold values from -6 to 6
- row_taps: float32 [16, 21], replicated, may hold values from -1 to 1
- col_taps: float32 [16, 21], replicated, may hold values from -1 to 1
- coeffs: float32 [16, 16, 6], P('visit'), may hold values from -2 to 2
- visits: float32 [16, 2048, 2048], P('visit', 'tile'), may hold values from -6 to 6
- boxes: int32 [16, 2], replicated, may hold values from 0 to 2048, as said below
Outputs:
- difference: float32 [16, 2048, 2048], P('visit', 'tile')
The draws below stay inside these ranges and needn't reach their ends.
Inputs may be any that keep to these rules, and one draw needn't show every extreme that they name: boxes[v, 0] is the first column and boxes[v, 1] the number of columns of visit v's box, which lies within the 2048 columns; boxes[v, 1] is at least 512, and some visit covers all 2048 columns.
All inputs are finite; a program needn't handle non-finite values.
Results may differ from the reference program's by a relative error of at most 0.0003.
Values sent between devices are 32-bit elements; how exact they have to be, the bound alone decides.
No kernel may reach another device: no remote copies, remote signals or barrier semaphores. Data moves between devices by JAX's collectives and lax.ppermute only.
A program may use at most 128 MiB of HBM per device.

```python
import jax
import jax.numpy as jnp
from jax import lax

W = 2048
K = 16
TAPS = 21
VISITS = 16
ROWS = 2048


def draw_boxes(key, part):
    first_key, second_key, third_key = jax.random.split(key, 3)
    lengths = jax.random.randint(first_key, (VISITS,), W // 4, W + 1)
    widest = jax.random.randint(second_key, (), 0, VISITS)
    lengths = jnp.where(jnp.arange(VISITS) == widest, W, lengths)
    starts = jax.random.randint(third_key, (VISITS,), 0, W) % (W - lengths + 1)
    return jnp.stack([starts, lengths], axis=1).astype(jnp.int32)


def steps_of(key, dims, cuts, low, largest):
    gain, own = 1.0, jax.random.fold_in(key, 6)
    for position, shards_of in cuts:
        draws = jnp.exp(jax.random.uniform(jax.random.fold_in(own, position), (shards_of,), jnp.float32, low / len(cuts), largest / len(cuts)))
        gain = gain * jnp.repeat(draws, dims[position] // shards_of).reshape([-1 if axis == position else 1 for axis in range(len(dims))])
    return gain


def gaussian(stream_key, dims, width, bound, cuts=(), dtype=jnp.bfloat16):
    loudness = steps_of(stream_key, dims, cuts, -0.22, 0.18) if cuts else 1.0
    entries = jax.random.normal(stream_key, dims, jnp.float32) * width * loudness
    return jnp.minimum(jnp.maximum(entries, -bound), bound).astype(dtype)


def setup_inputs(seed: int = 0) -> dict:
    streams_of = jax.random.split(jax.random.key(seed), 7)
    return {
        "template": gaussian(streams_of[0], (ROWS, W), 1.0, 6.0, ((0, 16), (1, 16)), jnp.float32),
        "row_taps": gaussian(streams_of[1], (K, TAPS), 0.22, 1.0, (), jnp.float32),
        "col_taps": gaussian(streams_of[2], (K, TAPS), 0.22, 1.0, (), jnp.float32),
        "coeffs": gaussian(streams_of[3], (VISITS, K, 6), 0.3, 2.0, ((0, 16),), jnp.float32),
        "visits": gaussian(streams_of[4], (VISITS, ROWS, W), 1.0, 6.0, ((0, 16), (1, 16)), jnp.float32),
        "boxes": draw_boxes(jax.random.fold_in(streams_of[6], 71), 0),
    }


def coordinate(first, count, total):
    return 2.0 * ((first + jnp.arange(count)).astype(jnp.float32) + 0.5) / total - 1.0


def surface_terms(y_coord, x_coord):
    y_grid = y_coord[:, None] * jnp.ones_like(x_coord)[None, :]
    x_grid = jnp.ones_like(y_coord)[:, None] * x_coord[None, :]
    return jnp.stack([jnp.ones_like(x_grid), x_grid, y_grid, x_grid * x_grid, x_grid * y_grid, y_grid * y_grid])


def separable(padded, row_taps, col_taps, tile_rows, span):
    passed = jnp.zeros((row_taps.shape[0], tile_rows, padded.shape[1]), jnp.float32)
    for offset in range(row_taps.shape[1]):
        passed = passed + row_taps[:, offset, None, None] * padded[None, offset:offset + tile_rows, :]
    images = jnp.zeros((row_taps.shape[0], tile_rows, span), jnp.float32)
    for offset in range(col_taps.shape[1]):
        images = images + col_taps[:, offset, None, None] * passed[:, :, offset:offset + span]
    return images


def reference(template, row_taps, col_taps, coeffs, visits, boxes):
    half = TAPS // 2
    padded = jnp.pad(template, half)
    basis = separable(padded, row_taps, col_taps, ROWS, W)
    terms = surface_terms(coordinate(0, ROWS, ROWS), coordinate(0, W, W))
    column_index = jnp.arange(W).astype(jnp.int32)

    def one_visit(packed):
        coef, visit, box = packed
        weighted = jnp.einsum("kt,krc->trc", coef, basis, precision=lax.Precision.HIGHEST)
        model = jnp.sum(weighted * terms, axis=0)
        inside = (column_index >= box[0]) & (column_index < box[0] + box[1])
        return jnp.where(inside[None, :], visit - model, jnp.float32(0.0))

    return lax.map(one_visit, (coeffs, visits, boxes))
```

```python
import jax
import jax.numpy as jnp
from jax import lax
from jax.sharding import PartitionSpec as P


def extended_2(cells, sides, width):
    for axis, dim in sides:
        count = lax.axis_size(axis)
        ends = count - 1
        head = lax.slice_in_dim(cells, 0, width, axis=dim)
        tail = lax.slice_in_dim(cells, cells.shape[dim] - width, cells.shape[dim], axis=dim)
        cells = jnp.concatenate(
            [
                lax.ppermute(tail, axis, [(i, (i + 1) % count) for i in range(ends)]),
                cells,
                lax.ppermute(head, axis, [((i + 1) % count, i) for i in range(ends)]),
            ],
            axis=dim,
        )
    return cells


def coordinate(first, count, total):
    return 2.0 * ((first + jnp.arange(count)).astype(jnp.float32) + 0.5) / total - 1.0


def surface_terms(y_coord, x_coord):
    y_grid = y_coord[:, None] * jnp.ones_like(x_coord)[None, :]
    x_grid = jnp.ones_like(y_coord)[:, None] * x_coord[None, :]
    return jnp.stack(
        [jnp.ones_like(x_grid), x_grid, y_grid, x_grid * x_grid, x_grid * y_grid, y_grid * y_grid]
    )


def separable(padded, row_taps, col_taps, tile_rows, span):
    passed = jnp.zeros((row_taps.shape[0], tile_rows, padded.shape[1]), jnp.float32)
    for offset in range(row_taps.shape[1]):
        passed = (
            passed + row_taps[:, offset, None, None] * padded[None, offset : offset + tile_rows, :]
        )
    images = jnp.zeros((row_taps.shape[0], tile_rows, span), jnp.float32)
    for offset in range(col_taps.shape[1]):
        images = images + col_taps[:, offset, None, None] * passed[:, :, offset : offset + span]
    return images


def combine(coef, images, y_coord, first_col, full_width):
    terms = surface_terms(y_coord, coordinate(first_col, images.shape[2], full_width))
    weighted = jnp.einsum("vkt,krc->vtrc", coef, images, precision=lax.Precision.HIGHEST)
    return jnp.sum(weighted * terms[None], axis=1)


def local(template, row_taps, col_taps, coeffs, visits, boxes):
    half = row_taps.shape[1] // 2
    tile_rows, columns = template.shape
    full_width = columns * lax.axis_size("visit")
    total_rows = tile_rows * lax.axis_size("tile")
    y_coord = coordinate(lax.axis_index("tile") * tile_rows, tile_rows, total_rows)
    visit_count = visits.shape[0]
    all_coeffs = lax.all_gather(coeffs, "visit", axis=0, tiled=True)
    extended = extended_2(template, (("tile", 0), ("visit", 1)), half)
    basis = separable(extended, row_taps, col_taps, tile_rows, columns)
    models = combine(all_coeffs, basis, y_coord, lax.axis_index("visit") * columns, full_width)
    model = lax.all_to_all(models, "visit", 0, 2, tiled=True)
    local_boxes = lax.dynamic_slice_in_dim(
        boxes, lax.axis_index("visit") * visit_count, visit_count, 0
    )
    column_index = jnp.arange(full_width)
    inside = (column_index[None, :] >= local_boxes[:, 0:1]) & (
        column_index[None, :] < local_boxes[:, 0:1] + local_boxes[:, 1:2]
    )
    return jnp.where(inside[:, None, :], visits - model, jnp.float32(0.0))


def solution(mesh):
    placed = (P("tile", "visit"), P(), P(), P("visit", None, None), P("visit", "tile", None), P())
    return jax.shard_map(
        local, mesh=mesh, in_specs=placed, out_specs=P("visit", "tile", None), check_vma=False
    )
```

```python
import jax
import jax.numpy as jnp
from jax import lax
from jax.sharding import PartitionSpec as P


def extended_2(cells, sides, width):
    for axis, dim in sides:
        count = lax.axis_size(axis)
        ends = count - 1
        head = lax.slice_in_dim(cells, 0, width, axis=dim)
        tail = lax.slice_in_dim(cells, cells.shape[dim] - width, cells.shape[dim], axis=dim)
        cells = jnp.concatenate(
            [
                lax.ppermute(tail, axis, [(i, (i + 1) % count) for i in range(ends)]),
                cells,
                lax.ppermute(head, axis, [((i + 1) % count, i) for i in range(ends)]),
            ],
            axis=dim,
        )
    return cells


def coordinate(first, count, total):
    return 2.0 * ((first + jnp.arange(count)).astype(jnp.float32) + 0.5) / total - 1.0


def surface_terms(y_coord, x_coord):
    y_grid = y_coord[:, None] * jnp.ones_like(x_coord)[None, :]
    x_grid = jnp.ones_like(y_coord)[:, None] * x_coord[None, :]
    return jnp.stack(
        [jnp.ones_like(x_grid), x_grid, y_grid, x_grid * x_grid, x_grid * y_grid, y_grid * y_grid]
    )


def separable(padded, row_taps, col_taps, tile_rows, span):
    passed = jnp.zeros((row_taps.shape[0], tile_rows, padded.shape[1]), jnp.float32)
    for offset in range(row_taps.shape[1]):
        passed = (
            passed + row_taps[:, offset, None, None] * padded[None, offset : offset + tile_rows, :]
        )
    images = jnp.zeros((row_taps.shape[0], tile_rows, span), jnp.float32)
    for offset in range(col_taps.shape[1]):
        images = images + col_taps[:, offset, None, None] * passed[:, :, offset : offset + span]
    return images


def combine(coef, images, y_coord, first_col, full_width):
    terms = surface_terms(y_coord, coordinate(first_col, images.shape[2], full_width))
    weighted = jnp.einsum("vkt,krc->vtrc", coef, images, precision=lax.Precision.HIGHEST)
    return jnp.sum(weighted * terms[None], axis=1)


def local(template, row_taps, col_taps, coeffs, visits, boxes):
    half = row_taps.shape[1] // 2
    tile_rows, columns = template.shape
    full_width = columns * lax.axis_size("visit")
    total_rows = tile_rows * lax.axis_size("tile")
    y_coord = coordinate(lax.axis_index("tile") * tile_rows, tile_rows, total_rows)
    visit_count = visits.shape[0]
    copies = jnp.broadcast_to(coeffs, (lax.axis_size("visit"),) + coeffs.shape[1:])
    all_coeffs = lax.all_to_all(copies, "visit", 0, 0, tiled=True)
    extended = extended_2(template, (("tile", 0), ("visit", 1)), half)
    basis = separable(extended, row_taps, col_taps, tile_rows, columns)
    models = combine(all_coeffs, basis, y_coord, lax.axis_index("visit") * columns, full_width)
    model = lax.all_to_all(models, "visit", 0, 2, tiled=True)
    local_boxes = lax.dynamic_slice_in_dim(
        boxes, lax.axis_index("visit") * visit_count, visit_count, 0
    )
    column_index = jnp.arange(full_width)
    inside = (column_index[None, :] >= local_boxes[:, 0:1]) & (
        column_index[None, :] < local_boxes[:, 0:1] + local_boxes[:, 1:2]
    )
    return jnp.where(inside[:, None, :], visits - model, jnp.float32(0.0))


def solution(mesh):
    placed = (P("tile", "visit"), P(), P(), P("visit", None, None), P("visit", "tile", None), P())
    return jax.shard_map(
        local, mesh=mesh, in_specs=placed, out_specs=P("visit", "tile", None), check_vma=False
    )
```

```python
import jax
import jax.numpy as jnp
from jax import lax
from jax.sharding import Mesh
from jax.sharding import PartitionSpec as P


def coordinate(first, count, total):
    return 2.0 * ((first + jnp.arange(count)).astype(jnp.float32) + 0.5) / total - 1.0


def surface_terms(y_coord, x_coord):
    y_grid = y_coord[:, None] * jnp.ones_like(x_coord)[None, :]
    x_grid = jnp.ones_like(y_coord)[:, None] * x_coord[None, :]
    return jnp.stack(
        [jnp.ones_like(x_grid), x_grid, y_grid, x_grid * x_grid, x_grid * y_grid, y_grid * y_grid]
    )


def separable(padded, row_taps, col_taps, tile_rows, span):
    passed = jnp.zeros((row_taps.shape[0], tile_rows, padded.shape[1]), jnp.float32)
    for offset in range(row_taps.shape[1]):
        passed = (
            passed + row_taps[:, offset, None, None] * padded[None, offset : offset + tile_rows, :]
        )
    images = jnp.zeros((row_taps.shape[0], tile_rows, span), jnp.float32)
    for offset in range(col_taps.shape[1]):
        images = images + col_taps[:, offset, None, None] * passed[:, :, offset : offset + span]
    return images


def local(template, row_taps, col_taps, coeffs, visits, boxes):
    half = row_taps.shape[1] // 2
    tile_rows, columns = template.shape
    tiles = lax.axis_size("tile")
    halves = lax.axis_size("zhi")
    group = lax.axis_size("xc")
    tile = lax.axis_index("tile")
    side = lax.axis_index("zhi")
    place = lax.axis_index("xc")
    full_width = columns * halves * group
    total_rows = tile_rows * tiles

    copies = jnp.broadcast_to(coeffs, (group,) + coeffs.shape[1:])
    half_coeffs = lax.all_to_all(copies, "xc", 0, 0, tiled=True)

    top = template[:half]
    bottom = template[tile_rows - half :]
    swap = [(h, halves - 1 - h) for h in range(halves)]
    partner = lax.ppermute(template, "zhi", swap)
    down = [(i, i + 1) for i in range(tiles - 1)]
    up = [(i + 1, i) for i in range(tiles - 1)]
    above = lax.ppermute(bottom, "tile", down)
    below = lax.ppermute(top, "tile", up)

    def crossed(pairs):
        return [(i * halves + h, j * halves + halves - 1 - h) for i, j in pairs for h in range(halves)]

    partner_above = lax.ppermute(bottom, ("tile", "zhi"), crossed(down))
    partner_below = lax.ppermute(top, ("tile", "zhi"), crossed(up))
    own = jnp.concatenate([above, template, below], axis=0)
    other = jnp.concatenate([partner_above, partner, partner_below], axis=0)
    first = side == 0
    blocks = jnp.stack([jnp.where(first, own, other), jnp.where(first, other, own)])
    blocks = jnp.pad(blocks, ((0, 0), (0, 0), (2 * half, 2 * half)))
    span = columns + 2 * half
    y_coord = coordinate(tile * tile_rows, tile_rows, total_rows)
    models = []
    for b in range(halves):
        basis = separable(blocks[b], row_taps, col_taps, tile_rows, span)
        start = (b * group + place) * columns - half
        terms = surface_terms(y_coord, coordinate(start, span, full_width))
        weighted = jnp.einsum("vkt,krc->vtrc", half_coeffs, basis, precision=lax.Precision.HIGHEST)
        models.append(jnp.sum(weighted * terms[None], axis=1))
    models = jnp.stack(models, axis=1)
    parts = lax.all_to_all(models, "xc", 0, 0, tiled=True)
    parts = jnp.swapaxes(parts, 0, 1).reshape((halves * group,) + parts.shape[2:])
    core = parts[:, :, half : half + columns]
    left = parts[:, :, :half]
    right = parts[:, :, half + columns :]
    edge = jnp.zeros_like(left[:1])
    core = core.at[:, :, :half].add(jnp.concatenate([edge, right[:-1]], axis=0))
    core = core.at[:, :, columns - half :].add(jnp.concatenate([left[1:], edge], axis=0))
    model = jnp.swapaxes(core, 0, 1).reshape(1, tile_rows, full_width)

    visit = side * group + place
    local_boxes = lax.dynamic_slice_in_dim(boxes, visit, 1, 0)
    column_index = jnp.arange(full_width)
    inside = (column_index[None, :] >= local_boxes[:, 0:1]) & (
        column_index[None, :] < local_boxes[:, 0:1] + local_boxes[:, 1:2]
    )
    return jnp.where(inside[:, None, :], visits - model, jnp.float32(0.0))


def solution(mesh):
    tiles, visits = mesh.devices.shape
    split = Mesh(mesh.devices.reshape(tiles, 2, visits // 2), ("tile", "zhi", "xc"))
    cols = ("zhi", "xc")
    placed = (P("tile", cols), P(), P(), P(cols, None, None), P(cols, "tile", None), P())
    return jax.shard_map(
        local, mesh=split, in_specs=placed, out_specs=P(cols, "tile", None), check_vma=False
    )
```

```python
import jax
import jax.numpy as jnp
from jax import lax
from jax.sharding import Mesh
from jax.sharding import PartitionSpec as P


def coordinate(first, count, total):
    return 2.0 * ((first + jnp.arange(count)).astype(jnp.float32) + 0.5) / total - 1.0


def surface_terms(y_coord, x_coord):
    y_grid = y_coord[:, None] * jnp.ones_like(x_coord)[None, :]
    x_grid = jnp.ones_like(y_coord)[:, None] * x_coord[None, :]
    return jnp.stack(
        [jnp.ones_like(x_grid), x_grid, y_grid, x_grid * x_grid, x_grid * y_grid, y_grid * y_grid]
    )


def banded(taps, rows, cols):
    offset = lax.broadcasted_iota(jnp.int32, (rows, cols), 1) - lax.broadcasted_iota(jnp.int32, (rows, cols), 0)
    band = jnp.zeros((taps.shape[0], rows, cols), jnp.float32)
    for tap in range(taps.shape[1]):
        band = band + jnp.where(offset == tap, taps[:, tap, None, None], jnp.float32(0.0))
    return band


def separable(blocks, row_taps, col_taps, tile_rows, span):
    reach = row_taps.shape[1]
    down = banded(row_taps, tile_rows, tile_rows + reach - 1)
    across = jnp.swapaxes(banded(col_taps, span, span + reach - 1), 1, 2)
    passed = jnp.einsum("kra,bac->bkrc", down, blocks, precision=lax.Precision.HIGHEST)
    return jnp.einsum("bkrc,kcd->bkrd", passed, across, precision=lax.Precision.HIGHEST)


def local(template, row_taps, col_taps, coeffs, visits, boxes):
    half = row_taps.shape[1] // 2
    tile_rows, columns = template.shape
    tiles = lax.axis_size("tile")
    halves = lax.axis_size("zhi")
    group = lax.axis_size("xc")
    tile = lax.axis_index("tile")
    side = lax.axis_index("zhi")
    place = lax.axis_index("xc")
    full_width = columns * halves * group
    total_rows = tile_rows * tiles

    copies = jnp.broadcast_to(coeffs, (group,) + coeffs.shape[1:])
    half_coeffs = lax.all_to_all(copies, "xc", 0, 0, tiled=True)

    top = template[:half]
    bottom = template[tile_rows - half :]
    swap = [(h, halves - 1 - h) for h in range(halves)]
    partner = lax.ppermute(template, "zhi", swap)
    down = [(i, i + 1) for i in range(tiles - 1)]
    up = [(i + 1, i) for i in range(tiles - 1)]
    above = lax.ppermute(bottom, "tile", down)
    below = lax.ppermute(top, "tile", up)

    def crossed(pairs):
        return [(i * halves + h, j * halves + halves - 1 - h) for i, j in pairs for h in range(halves)]

    partner_above = lax.ppermute(bottom, ("tile", "zhi"), crossed(down))
    partner_below = lax.ppermute(top, ("tile", "zhi"), crossed(up))
    own = jnp.concatenate([above, template, below], axis=0)
    other = jnp.concatenate([partner_above, partner, partner_below], axis=0)
    first = side == 0
    blocks = jnp.stack([jnp.where(first, own, other), jnp.where(first, other, own)])
    blocks = jnp.pad(blocks, ((0, 0), (0, 0), (2 * half, 2 * half)))
    span = columns + 2 * half
    y_coord = coordinate(tile * tile_rows, tile_rows, total_rows)
    basis = separable(blocks, row_taps, col_taps, tile_rows, span)
    models = []
    for b in range(halves):
        start = (b * group + place) * columns - half
        terms = surface_terms(y_coord, coordinate(start, span, full_width))
        weighted = jnp.einsum("vkt,krc->vtrc", half_coeffs, basis[b], precision=lax.Precision.HIGHEST)
        models.append(jnp.sum(weighted * terms[None], axis=1))
    models = jnp.stack(models, axis=1)
    parts = lax.all_to_all(models, "xc", 0, 0, tiled=True)
    parts = jnp.swapaxes(parts, 0, 1).reshape((halves * group,) + parts.shape[2:])
    core = parts[:, :, half : half + columns]
    left = parts[:, :, :half]
    right = parts[:, :, half + columns :]
    edge = jnp.zeros_like(left[:1])
    core = core.at[:, :, :half].add(jnp.concatenate([edge, right[:-1]], axis=0))
    core = core.at[:, :, columns - half :].add(jnp.concatenate([left[1:], edge], axis=0))
    model = jnp.swapaxes(core, 0, 1).reshape(1, tile_rows, full_width)

    visit = side * group + place
    local_boxes = lax.dynamic_slice_in_dim(boxes, visit, 1, 0)
    column_index = jnp.arange(full_width)
    inside = (column_index[None, :] >= local_boxes[:, 0:1]) & (
        column_index[None, :] < local_boxes[:, 0:1] + local_boxes[:, 1:2]
    )
    return jnp.where(inside[:, None, :], visits - model, jnp.float32(0.0))


def solution(mesh):
    tiles, visits = mesh.devices.shape
    split = Mesh(mesh.devices.reshape(tiles, 2, visits // 2), ("tile", "zhi", "xc"))
    cols = ("zhi", "xc")
    placed = (P("tile", cols), P(), P(), P(cols, None, None), P(cols, "tile", None), P())
    return jax.shard_map(
        local, mesh=split, in_specs=placed, out_specs=P(cols, "tile", None), check_vma=False
    )
```

```python
import jax
import jax.numpy as jnp
from jax import lax
from jax.sharding import Mesh
from jax.sharding import PartitionSpec as P


def coordinate(first, count, total):
    return 2.0 * ((first + jnp.arange(count)).astype(jnp.float32) + 0.5) / total - 1.0


def surface_terms(y_coord, x_coord):
    y_grid = y_coord[:, None] * jnp.ones_like(x_coord)[None, :]
    x_grid = jnp.ones_like(y_coord)[:, None] * x_coord[None, :]
    return jnp.stack(
        [jnp.ones_like(x_grid), x_grid, y_grid, x_grid * x_grid, x_grid * y_grid, y_grid * y_grid]
    )


def banded(taps, rows, cols):
    offset = lax.broadcasted_iota(jnp.int32, (rows, cols), 1) - lax.broadcasted_iota(jnp.int32, (rows, cols), 0)
    picks = (offset[None] == jnp.arange(taps.shape[1])[:, None, None]).astype(jnp.float32)
    return jnp.einsum("ka,arc->krc", taps, picks, precision=lax.Precision.HIGHEST)


def separable(blocks, row_taps, col_taps, tile_rows, span):
    reach = row_taps.shape[1]
    down = banded(row_taps, tile_rows, tile_rows + reach - 1)
    across = jnp.swapaxes(banded(col_taps, span, span + reach - 1), 1, 2)
    passed = jnp.einsum("kra,bac->bkrc", down, blocks, precision=lax.Precision.HIGH)
    return jnp.einsum("bkrc,kcd->bkrd", passed, across, precision=lax.Precision.HIGH)


def local(template, row_taps, col_taps, coeffs, visits, boxes):
    half = row_taps.shape[1] // 2
    tile_rows, columns = template.shape
    tiles = lax.axis_size("tile")
    halves = lax.axis_size("zhi")
    group = lax.axis_size("xc")
    tile = lax.axis_index("tile")
    side = lax.axis_index("zhi")
    place = lax.axis_index("xc")
    full_width = columns * halves * group
    total_rows = tile_rows * tiles

    copies = jnp.broadcast_to(coeffs, (group,) + coeffs.shape[1:])
    half_coeffs = lax.all_to_all(copies, "xc", 0, 0, tiled=True)

    top = template[:half]
    bottom = template[tile_rows - half :]
    swap = [(h, halves - 1 - h) for h in range(halves)]
    partner = lax.ppermute(template, "zhi", swap)
    down = [(i, i + 1) for i in range(tiles - 1)]
    up = [(i + 1, i) for i in range(tiles - 1)]
    above = lax.ppermute(bottom, "tile", down)
    below = lax.ppermute(top, "tile", up)

    def crossed(pairs):
        return [(i * halves + h, j * halves + halves - 1 - h) for i, j in pairs for h in range(halves)]

    partner_above = lax.ppermute(bottom, ("tile", "zhi"), crossed(down))
    partner_below = lax.ppermute(top, ("tile", "zhi"), crossed(up))
    own = jnp.concatenate([above, template, below], axis=0)
    other = jnp.concatenate([partner_above, partner, partner_below], axis=0)
    first = side == 0
    blocks = jnp.stack([jnp.where(first, own, other), jnp.where(first, other, own)])
    blocks = jnp.pad(blocks, ((0, 0), (0, 0), (2 * half, 2 * half)))
    span = columns + 2 * half
    y_coord = coordinate(tile * tile_rows, tile_rows, total_rows)
    basis = separable(blocks, row_taps, col_taps, tile_rows, span)
    models = []
    y = y_coord[:, None]
    for b in range(halves):
        start = (b * group + place) * columns - half
        x = coordinate(start, span, full_width)[None, :]
        w = jnp.einsum("vkt,krc->tvrc", half_coeffs, basis[b], precision=lax.Precision.HIGH)
        models.append(w[0] + x * w[1] + y * w[2] + (x * x) * w[3] + (x * y) * w[4] + (y * y) * w[5])
    models = jnp.stack(models, axis=1)
    parts = lax.all_to_all(models, "xc", 0, 0, tiled=True)
    parts = jnp.swapaxes(parts, 0, 1).reshape((halves * group,) + parts.shape[2:])
    core = parts[:, :, half : half + columns]
    left = parts[:, :, :half]
    right = parts[:, :, half + columns :]
    edge = jnp.zeros_like(left[:1])
    core = core.at[:, :, :half].add(jnp.concatenate([edge, right[:-1]], axis=0))
    core = core.at[:, :, columns - half :].add(jnp.concatenate([left[1:], edge], axis=0))
    model = jnp.swapaxes(core, 0, 1).reshape(1, tile_rows, full_width)

    visit = side * group + place
    local_boxes = lax.dynamic_slice_in_dim(boxes, visit, 1, 0)
    column_index = jnp.arange(full_width)
    inside = (column_index[None, :] >= local_boxes[:, 0:1]) & (
        column_index[None, :] < local_boxes[:, 0:1] + local_boxes[:, 1:2]
    )
    return jnp.where(inside[:, None, :], visits - model, jnp.float32(0.0))


def solution(mesh):
    tiles, visits = mesh.devices.shape
    split = Mesh(mesh.devices.reshape(tiles, 2, visits // 2), ("tile", "zhi", "xc"))
    cols = ("zhi", "xc")
    placed = (P("tile", cols), P(), P(), P(cols, None, None), P(cols, "tile", None), P())
    return jax.shard_map(
        local, mesh=split, in_specs=placed, out_specs=P(cols, "tile", None), check_vma=False
    )
```

```python
import jax
import jax.numpy as jnp
from jax import lax
from jax.sharding import Mesh
from jax.sharding import PartitionSpec as P


def coordinate(first, count, total):
    return 2.0 * ((first + jnp.arange(count)).astype(jnp.float32) + 0.5) / total - 1.0


def surface_terms(y_coord, x_coord):
    y_grid = y_coord[:, None] * jnp.ones_like(x_coord)[None, :]
    x_grid = jnp.ones_like(y_coord)[:, None] * x_coord[None, :]
    return jnp.stack(
        [jnp.ones_like(x_grid), x_grid, y_grid, x_grid * x_grid, x_grid * y_grid, y_grid * y_grid]
    )


def banded(row_taps, col_taps, rows, cols):
    offset = lax.broadcasted_iota(jnp.int32, (rows, cols), 1) - lax.broadcasted_iota(jnp.int32, (rows, cols), 0)
    picks = (offset[None] == jnp.arange(row_taps.shape[1])[:, None, None]).astype(jnp.float32)
    taps = jnp.concatenate([row_taps, col_taps], axis=0)
    return jnp.einsum("ka,arc->krc", taps, picks, precision=lax.Precision.HIGHEST)


def separable(blocks, row_taps, col_taps, tile_rows, span):
    kernels, reach = row_taps.shape
    bands = banded(row_taps, col_taps, span, span + reach - 1)
    down = bands[:kernels, :tile_rows, : tile_rows + reach - 1]
    across = jnp.swapaxes(bands[kernels:], 1, 2)
    passed = jnp.einsum("kra,bac->bkrc", down, blocks, precision=lax.Precision.HIGH)
    return jnp.einsum("bkrc,kcd->bkrd", passed, across, precision=lax.Precision.HIGH)


def local(template, row_taps, col_taps, coeffs, visits, boxes):
    half = row_taps.shape[1] // 2
    tile_rows, columns = template.shape
    tiles = lax.axis_size("tile")
    halves = lax.axis_size("zhi")
    group = lax.axis_size("xc")
    tile = lax.axis_index("tile")
    side = lax.axis_index("zhi")
    place = lax.axis_index("xc")
    full_width = columns * halves * group
    total_rows = tile_rows * tiles

    copies = jnp.broadcast_to(coeffs, (group,) + coeffs.shape[1:])
    half_coeffs = lax.all_to_all(copies, "xc", 0, 0, tiled=True)

    top = template[:half]
    bottom = template[tile_rows - half :]
    down = [(i, i + 1) for i in range(tiles - 1)]
    up = [(i + 1, i) for i in range(tiles - 1)]
    above = lax.ppermute(bottom, "tile", down)
    below = lax.ppermute(top, "tile", up)
    own = jnp.concatenate([above, template, below], axis=0)
    swap = [(h, halves - 1 - h) for h in range(halves)]
    other = lax.ppermute(own, "zhi", swap)
    first = side == 0
    blocks = jnp.stack([jnp.where(first, own, other), jnp.where(first, other, own)])
    blocks = jnp.pad(blocks, ((0, 0), (0, 0), (2 * half, 2 * half)))
    span = columns + 2 * half
    y_coord = coordinate(tile * tile_rows, tile_rows, total_rows)
    basis = separable(blocks, row_taps, col_taps, tile_rows, span)
    models = []
    y = y_coord[:, None]
    for b in range(halves):
        start = (b * group + place) * columns - half
        x = coordinate(start, span, full_width)[None, :]
        w = jnp.einsum("vkt,krc->tvrc", half_coeffs, basis[b], precision=lax.Precision.HIGH)
        models.append(w[0] + x * w[1] + y * w[2] + (x * x) * w[3] + (x * y) * w[4] + (y * y) * w[5])
    models = jnp.stack(models, axis=1)
    parts = lax.all_to_all(models, "xc", 0, 0, tiled=True)
    parts = jnp.swapaxes(parts, 0, 1).reshape((halves * group,) + parts.shape[2:])
    core = parts[:, :, half : half + columns]
    left = parts[:, :, :half]
    right = parts[:, :, half + columns :]
    edge = jnp.zeros_like(left[:1])
    core = core.at[:, :, :half].add(jnp.concatenate([edge, right[:-1]], axis=0))
    core = core.at[:, :, columns - half :].add(jnp.concatenate([left[1:], edge], axis=0))
    model = jnp.swapaxes(core, 0, 1).reshape(1, tile_rows, full_width)

    visit = side * group + place
    local_boxes = lax.dynamic_slice_in_dim(boxes, visit, 1, 0)
    column_index = jnp.arange(full_width)
    inside = (column_index[None, :] >= local_boxes[:, 0:1]) & (
        column_index[None, :] < local_boxes[:, 0:1] + local_boxes[:, 1:2]
    )
    return jnp.where(inside[:, None, :], visits - model, jnp.float32(0.0))


def solution(mesh):
    tiles, visits = mesh.devices.shape
    split = Mesh(mesh.devices.reshape(tiles, 2, visits // 2), ("tile", "zhi", "xc"))
    cols = ("zhi", "xc")
    placed = (P("tile", cols), P(), P(), P(cols, None, None), P(cols, "tile", None), P())
    return jax.shard_map(
        local, mesh=split, in_specs=placed, out_specs=P(cols, "tile", None), check_vma=False
    )
```

```python
import jax
import jax.numpy as jnp
from jax import lax
from jax.sharding import Mesh
from jax.sharding import PartitionSpec as P


def coordinate(first, count, total):
    return 2.0 * ((first + jnp.arange(count)).astype(jnp.float32) + 0.5) / total - 1.0


def surface_terms(y_coord, x_coord):
    y_grid = y_coord[:, None] * jnp.ones_like(x_coord)[None, :]
    x_grid = jnp.ones_like(y_coord)[:, None] * x_coord[None, :]
    return jnp.stack(
        [jnp.ones_like(x_grid), x_grid, y_grid, x_grid * x_grid, x_grid * y_grid, y_grid * y_grid]
    )


def banded(row_taps, col_taps, rows, cols):
    offset = lax.broadcasted_iota(jnp.int32, (rows, cols), 1) - lax.broadcasted_iota(jnp.int32, (rows, cols), 0)
    picks = (offset[None] == jnp.arange(row_taps.shape[1])[:, None, None]).astype(jnp.float32)
    taps = jnp.concatenate([row_taps, col_taps], axis=0)
    return jnp.einsum("ka,arc->krc", taps, picks, precision=lax.Precision.HIGHEST)


def separable(block, down, across):
    passed = jnp.einsum("kra,ac->krc", down, block, precision=lax.Precision.HIGH)
    return jnp.einsum("krc,kcd->krd", passed, across, precision=lax.Precision.HIGH)


def local(template, row_taps, col_taps, coeffs, visits, boxes):
    half = row_taps.shape[1] // 2
    tile_rows, columns = template.shape
    tiles = lax.axis_size("tile")
    halves = lax.axis_size("zhi")
    group = lax.axis_size("xc")
    tile = lax.axis_index("tile")
    side = lax.axis_index("zhi")
    place = lax.axis_index("xc")
    full_width = columns * halves * group
    total_rows = tile_rows * tiles

    copies = jnp.broadcast_to(coeffs, (group,) + coeffs.shape[1:])
    half_coeffs = lax.all_to_all(copies, "xc", 0, 0, tiled=True)

    top = template[:half]
    bottom = template[tile_rows - half :]
    down = [(i, i + 1) for i in range(tiles - 1)]
    up = [(i + 1, i) for i in range(tiles - 1)]
    above = lax.ppermute(bottom, "tile", down)
    below = lax.ppermute(top, "tile", up)
    own = jnp.concatenate([above, template, below], axis=0)
    swap = [(h, halves - 1 - h) for h in range(halves)]
    other = lax.ppermute(own, "zhi", swap)
    first = side == 0
    span = columns + 2 * half
    y_coord = coordinate(tile * tile_rows, tile_rows, total_rows)
    kernels, reach = row_taps.shape
    bands = banded(row_taps, col_taps, span, span + reach - 1)
    down = bands[:kernels, :tile_rows, : tile_rows + reach - 1]
    across = jnp.swapaxes(bands[kernels:], 1, 2)
    models = []
    y = y_coord[:, None]
    for b, block in enumerate((own, other)):
        block = jnp.pad(block, ((0, 0), (2 * half, 2 * half)))
        basis = separable(block, down, across)
        source = side if b == 0 else halves - 1 - side
        start = (source * group + place) * columns - half
        x = coordinate(start, span, full_width)[None, :]
        w = jnp.einsum("vkt,krc->tvrc", half_coeffs, basis, precision=lax.Precision.HIGH)
        models.append(w[0] + x * w[1] + y * w[2] + (x * x) * w[3] + (x * y) * w[4] + (y * y) * w[5])
    models = jnp.stack(models, axis=1)
    parts = lax.all_to_all(models, "xc", 0, 0, tiled=True)
    parts = jnp.where(first, parts, parts[:, ::-1])
    parts = jnp.swapaxes(parts, 0, 1).reshape((halves * group,) + parts.shape[2:])
    core = parts[:, :, half : half + columns]
    left = parts[:, :, :half]
    right = parts[:, :, half + columns :]
    edge = jnp.zeros_like(left[:1])
    core = core.at[:, :, :half].add(jnp.concatenate([edge, right[:-1]], axis=0))
    core = core.at[:, :, columns - half :].add(jnp.concatenate([left[1:], edge], axis=0))
    model = jnp.swapaxes(core, 0, 1).reshape(1, tile_rows, full_width)

    visit = side * group + place
    local_boxes = lax.dynamic_slice_in_dim(boxes, visit, 1, 0)
    column_index = jnp.arange(full_width)
    inside = (column_index[None, :] >= local_boxes[:, 0:1]) & (
        column_index[None, :] < local_boxes[:, 0:1] + local_boxes[:, 1:2]
    )
    return jnp.where(inside[:, None, :], visits - model, jnp.float32(0.0))


def solution(mesh):
    tiles, visits = mesh.devices.shape
    split = Mesh(mesh.devices.reshape(tiles, 2, visits // 2), ("tile", "zhi", "xc"))
    cols = ("zhi", "xc")
    placed = (P("tile", cols), P(), P(), P(cols, None, None), P(cols, "tile", None), P())
    return jax.shard_map(
        local, mesh=split, in_specs=placed, out_specs=P(cols, "tile", None), check_vma=False
    )
```

```python
import jax
import jax.numpy as jnp
from jax import lax
from jax.sharding import Mesh
from jax.sharding import PartitionSpec as P


def coordinate(first, count, total):
    return 2.0 * ((first + jnp.arange(count)).astype(jnp.float32) + 0.5) / total - 1.0


def surface_terms(y_coord, x_coord):
    y_grid = y_coord[:, None] * jnp.ones_like(x_coord)[None, :]
    x_grid = jnp.ones_like(y_coord)[:, None] * x_coord[None, :]
    return jnp.stack(
        [jnp.ones_like(x_grid), x_grid, y_grid, x_grid * x_grid, x_grid * y_grid, y_grid * y_grid]
    )


def banded(row_taps, col_taps, rows, cols):
    offset = lax.broadcasted_iota(jnp.int32, (rows, cols), 1) - lax.broadcasted_iota(jnp.int32, (rows, cols), 0)
    picks = (offset[None] == jnp.arange(row_taps.shape[1])[:, None, None]).astype(jnp.float32)
    taps = jnp.concatenate([row_taps, col_taps], axis=0)
    return jnp.einsum("ka,arc->krc", taps, picks, precision=lax.Precision.HIGHEST)


def separable(blocks, row_taps, col_taps, tile_rows, span):
    kernels, reach = row_taps.shape
    bands = banded(row_taps, col_taps, span, span + reach - 1)
    down = bands[:kernels, :tile_rows, : tile_rows + reach - 1]
    across = jnp.swapaxes(bands[kernels:], 1, 2)
    passed = jnp.einsum("kra,bac->bkrc", down, blocks, precision=lax.Precision.HIGH)
    return jnp.einsum("bkrc,kcd->bkrd", passed, across, precision=lax.Precision.HIGH)


def local(template, row_taps, col_taps, coeffs, visits, boxes):
    half = row_taps.shape[1] // 2
    tile_rows, columns = template.shape
    tiles = lax.axis_size("tile")
    halves = lax.axis_size("zhi")
    group = lax.axis_size("xc")
    tile = lax.axis_index("tile")
    side = lax.axis_index("zhi")
    place = lax.axis_index("xc")
    full_width = columns * halves * group
    total_rows = tile_rows * tiles

    copies = jnp.broadcast_to(coeffs, (group,) + coeffs.shape[1:])
    half_coeffs = lax.all_to_all(copies, "xc", 0, 0, tiled=True)

    swap = [(h, halves - 1 - h) for h in range(halves)]
    pair = jnp.stack([template, lax.ppermute(template, "zhi", swap)])
    down = [(i, i + 1) for i in range(tiles - 1)]
    up = [(i + 1, i) for i in range(tiles - 1)]
    above = lax.ppermute(pair[:, tile_rows - half :], "tile", down)
    below = lax.ppermute(pair[:, :half], "tile", up)
    extended = jnp.concatenate([above, pair, below], axis=1)
    own = extended[0]
    other = extended[1]
    first = side == 0
    blocks = jnp.stack([jnp.where(first, own, other), jnp.where(first, other, own)])
    blocks = jnp.pad(blocks, ((0, 0), (0, 0), (2 * half, 2 * half)))
    span = columns + 2 * half
    y_coord = coordinate(tile * tile_rows, tile_rows, total_rows)
    basis = separable(blocks, row_taps, col_taps, tile_rows, span)
    models = []
    y = y_coord[:, None]
    for b in range(halves):
        start = (b * group + place) * columns - half
        x = coordinate(start, span, full_width)[None, :]
        w = jnp.einsum("vkt,krc->tvrc", half_coeffs, basis[b], precision=lax.Precision.HIGH)
        models.append(w[0] + x * w[1] + y * w[2] + (x * x) * w[3] + (x * y) * w[4] + (y * y) * w[5])
    models = jnp.stack(models, axis=1)
    parts = lax.all_to_all(models, "xc", 0, 0, tiled=True)
    parts = jnp.swapaxes(parts, 0, 1).reshape((halves * group,) + parts.shape[2:])
    core = parts[:, :, half : half + columns]
    left = parts[:, :, :half]
    right = parts[:, :, half + columns :]
    edge = jnp.zeros_like(left[:1])
    core = core.at[:, :, :half].add(jnp.concatenate([edge, right[:-1]], axis=0))
    core = core.at[:, :, columns - half :].add(jnp.concatenate([left[1:], edge], axis=0))
    model = jnp.swapaxes(core, 0, 1).reshape(1, tile_rows, full_width)

    visit = side * group + place
    local_boxes = lax.dynamic_slice_in_dim(boxes, visit, 1, 0)
    column_index = jnp.arange(full_width)
    inside = (column_index[None, :] >= local_boxes[:, 0:1]) & (
        column_index[None, :] < local_boxes[:, 0:1] + local_boxes[:, 1:2]
    )
    return jnp.where(inside[:, None, :], visits - model, jnp.float32(0.0))


def solution(mesh):
    tiles, visits = mesh.devices.shape
    split = Mesh(mesh.devices.reshape(tiles, 2, visits // 2), ("tile", "zhi", "xc"))
    cols = ("zhi", "xc")
    placed = (P("tile", cols), P(), P(), P(cols, None, None), P(cols, "tile", None), P())
    return jax.shard_map(
        local, mesh=split, in_specs=placed, out_specs=P(cols, "tile", None), check_vma=False
    )
```

```python
import jax
import jax.numpy as jnp
from jax import lax
from jax.sharding import Mesh
from jax.sharding import PartitionSpec as P


def coordinate(first, count, total):
    return 2.0 * ((first + jnp.arange(count)).astype(jnp.float32) + 0.5) / total - 1.0


def surface_terms(y_coord, x_coord):
    y_grid = y_coord[:, None] * jnp.ones_like(x_coord)[None, :]
    x_grid = jnp.ones_like(y_coord)[:, None] * x_coord[None, :]
    return jnp.stack(
        [jnp.ones_like(x_grid), x_grid, y_grid, x_grid * x_grid, x_grid * y_grid, y_grid * y_grid]
    )


def banded(row_taps, col_taps, rows, cols):
    offset = lax.broadcasted_iota(jnp.int32, (rows, cols), 1) - lax.broadcasted_iota(jnp.int32, (rows, cols), 0)
    picks = (offset[None] == jnp.arange(row_taps.shape[1])[:, None, None]).astype(jnp.float32)
    taps = jnp.concatenate([row_taps, col_taps], axis=0)
    return jnp.einsum("ka,arc->krc", taps, picks, precision=lax.Precision.HIGH)


def separable(blocks, row_taps, col_taps, tile_rows, span):
    kernels, reach = row_taps.shape
    bands = banded(row_taps, col_taps, span, span + reach - 1)
    down = bands[:kernels, :tile_rows, : tile_rows + reach - 1]
    across = jnp.swapaxes(bands[kernels:], 1, 2)
    passed = jnp.einsum("kra,bac->bkrc", down, blocks, precision=lax.Precision.HIGH)
    return jnp.einsum("bkrc,kcd->bkrd", passed, across, precision=lax.Precision.HIGH)


def local(template, row_taps, col_taps, coeffs, visits, boxes):
    half = row_taps.shape[1] // 2
    tile_rows, columns = template.shape
    tiles = lax.axis_size("tile")
    halves = lax.axis_size("zhi")
    group = lax.axis_size("xc")
    tile = lax.axis_index("tile")
    side = lax.axis_index("zhi")
    place = lax.axis_index("xc")
    full_width = columns * halves * group
    total_rows = tile_rows * tiles

    copies = jnp.broadcast_to(coeffs, (group,) + coeffs.shape[1:])
    half_coeffs = lax.all_to_all(copies, "xc", 0, 0, tiled=True)

    swap = [(h, halves - 1 - h) for h in range(halves)]
    pair = jnp.stack([template, lax.ppermute(template, "zhi", swap)])
    down = [(i, i + 1) for i in range(tiles - 1)]
    up = [(i + 1, i) for i in range(tiles - 1)]
    above = lax.ppermute(pair[:, tile_rows - half :], "tile", down)
    below = lax.ppermute(pair[:, :half], "tile", up)
    extended = jnp.concatenate([above, pair, below], axis=1)
    own = extended[0]
    other = extended[1]
    first = side == 0
    blocks = jnp.stack([jnp.where(first, own, other), jnp.where(first, other, own)])
    blocks = jnp.pad(blocks, ((0, 0), (0, 0), (2 * half, 2 * half)))
    span = columns + 2 * half
    y_coord = coordinate(tile * tile_rows, tile_rows, total_rows)
    basis = separable(blocks, row_taps, col_taps, tile_rows, span)
    y = y_coord[None, None, :, None]
    starts = (jnp.arange(halves) * group + place) * columns - half
    x = jnp.stack([coordinate(start, span, full_width) for start in starts])[None, :, None, :]
    w = jnp.einsum("vkt,bkrc->tvbrc", half_coeffs, basis, precision=lax.Precision.HIGH)
    models = w[0] + x * w[1] + y * w[2] + (x * x) * w[3] + (x * y) * w[4] + (y * y) * w[5]
    parts = lax.all_to_all(models, "xc", 0, 0, tiled=True)
    parts = jnp.swapaxes(parts, 0, 1).reshape((halves * group,) + parts.shape[2:])
    core = parts[:, :, half : half + columns]
    left = parts[:, :, :half]
    right = parts[:, :, half + columns :]
    edge = jnp.zeros_like(left[:1])
    core = core.at[:, :, :half].add(jnp.concatenate([edge, right[:-1]], axis=0))
    core = core.at[:, :, columns - half :].add(jnp.concatenate([left[1:], edge], axis=0))
    model = jnp.swapaxes(core, 0, 1).reshape(1, tile_rows, full_width)

    visit = side * group + place
    local_boxes = lax.dynamic_slice_in_dim(boxes, visit, 1, 0)
    column_index = jnp.arange(full_width)
    inside = (column_index[None, :] >= local_boxes[:, 0:1]) & (
        column_index[None, :] < local_boxes[:, 0:1] + local_boxes[:, 1:2]
    )
    return jnp.where(inside[:, None, :], visits - model, jnp.float32(0.0))


def solution(mesh):
    tiles, visits = mesh.devices.shape
    split = Mesh(mesh.devices.reshape(tiles, 2, visits // 2), ("tile", "zhi", "xc"))
    cols = ("zhi", "xc")
    placed = (P("tile", cols), P(), P(), P(cols, None, None), P(cols, "tile", None), P())
    return jax.shard_map(
        local, mesh=split, in_specs=placed, out_specs=P(cols, "tile", None), check_vma=False
    )
```

```python
import jax
import jax.numpy as jnp
from jax import lax
from jax.sharding import Mesh
from jax.sharding import PartitionSpec as P


def coordinate(first, count, total):
    return 2.0 * ((first + jnp.arange(count)).astype(jnp.float32) + 0.5) / total - 1.0


def surface_terms(y_coord, x_coord):
    y_grid = y_coord[:, None] * jnp.ones_like(x_coord)[None, :]
    x_grid = jnp.ones_like(y_coord)[:, None] * x_coord[None, :]
    return jnp.stack(
        [jnp.ones_like(x_grid), x_grid, y_grid, x_grid * x_grid, x_grid * y_grid, y_grid * y_grid]
    )


def banded(taps, rows, cols):
    offset = lax.broadcasted_iota(jnp.int32, (rows, cols), 1) - lax.broadcasted_iota(jnp.int32, (rows, cols), 0)
    picks = (offset[None] == jnp.arange(taps.shape[1])[:, None, None]).astype(jnp.float32)
    return jnp.einsum("ka,arc->krc", taps, picks, precision=lax.Precision.HIGHEST)


def separable(blocks, row_taps, col_taps, tile_rows, span):
    reach = row_taps.shape[1]
    down = banded(row_taps, tile_rows, tile_rows + reach - 1)
    across = jnp.swapaxes(banded(col_taps, span, span + reach - 1), 1, 2)
    passed = jnp.einsum("kra,bac->bkrc", down, blocks, precision=lax.Precision.HIGH)
    return jnp.einsum("bkrc,kcd->bkrd", passed, across, precision=lax.Precision.HIGH)


def local(template, row_taps, col_taps, coeffs, visits, boxes):
    half = row_taps.shape[1] // 2
    tile_rows, columns = template.shape
    tiles = lax.axis_size("tile")
    halves = lax.axis_size("zhi")
    group = lax.axis_size("xc")
    tile = lax.axis_index("tile")
    side = lax.axis_index("zhi")
    place = lax.axis_index("xc")
    full_width = columns * halves * group
    total_rows = tile_rows * tiles

    copies = jnp.broadcast_to(coeffs, (group,) + coeffs.shape[1:])
    half_coeffs = lax.all_to_all(copies, "xc", 0, 0, tiled=True)

    swap = [(h, halves - 1 - h) for h in range(halves)]
    pair = jnp.stack([template, lax.ppermute(template, "zhi", swap)])
    down = [(i, i + 1) for i in range(tiles - 1)]
    up = [(i + 1, i) for i in range(tiles - 1)]
    above = lax.ppermute(pair[:, tile_rows - half :], "tile", down)
    below = lax.ppermute(pair[:, :half], "tile", up)
    extended = jnp.concatenate([above, pair, below], axis=1)
    own = extended[0]
    other = extended[1]
    first = side == 0
    blocks = jnp.stack([jnp.where(first, own, other), jnp.where(first, other, own)])
    blocks = jnp.pad(blocks, ((0, 0), (0, 0), (2 * half, 2 * half)))
    span = columns + 2 * half
    y_coord = coordinate(tile * tile_rows, tile_rows, total_rows)
    basis = separable(blocks, row_taps, col_taps, tile_rows, span)
    models = []
    y = y_coord[:, None]
    for b in range(halves):
        start = (b * group + place) * columns - half
        x = coordinate(start, span, full_width)[None, :]
        w = jnp.einsum("vkt,krc->tvrc", half_coeffs, basis[b], precision=lax.Precision.HIGH)
        models.append(w[0] + x * w[1] + y * w[2] + (x * x) * w[3] + (x * y) * w[4] + (y * y) * w[5])
    models = jnp.stack(models, axis=1)
    parts = lax.all_to_all(models, "xc", 0, 0, tiled=True)
    parts = jnp.swapaxes(parts, 0, 1).reshape((halves * group,) + parts.shape[2:])
    core = parts[:, :, half : half + columns]
    left = parts[:, :, :half]
    right = parts[:, :, half + columns :]
    edge = jnp.zeros_like(left[:1])
    core = core.at[:, :, :half].add(jnp.concatenate([edge, right[:-1]], axis=0))
    core = core.at[:, :, columns - half :].add(jnp.concatenate([left[1:], edge], axis=0))
    model = jnp.swapaxes(core, 0, 1).reshape(1, tile_rows, full_width)

    visit = side * group + place
    local_boxes = lax.dynamic_slice_in_dim(boxes, visit, 1, 0)
    column_index = jnp.arange(full_width)
    inside = (column_index[None, :] >= local_boxes[:, 0:1]) & (
        column_index[None, :] < local_boxes[:, 0:1] + local_boxes[:, 1:2]
    )
    return jnp.where(inside[:, None, :], visits - model, jnp.float32(0.0))


def solution(mesh):
    tiles, visits = mesh.devices.shape
    split = Mesh(mesh.devices.reshape(tiles, 2, visits // 2), ("tile", "zhi", "xc"))
    cols = ("zhi", "xc")
    placed = (P("tile", cols), P(), P(), P(cols, None, None), P(cols, "tile", None), P())
    return jax.shard_map(
        local, mesh=split, in_specs=placed, out_specs=P(cols, "tile", None), check_vma=False
    )
```

```python
import jax
import jax.numpy as jnp
from jax import lax
from jax.sharding import Mesh
from jax.sharding import PartitionSpec as P


def coordinate(first, count, total):
    return 2.0 * ((first + jnp.arange(count)).astype(jnp.float32) + 0.5) / total - 1.0


def surface_terms(y_coord, x_coord):
    y_grid = y_coord[:, None] * jnp.ones_like(x_coord)[None, :]
    x_grid = jnp.ones_like(y_coord)[:, None] * x_coord[None, :]
    return jnp.stack(
        [jnp.ones_like(x_grid), x_grid, y_grid, x_grid * x_grid, x_grid * y_grid, y_grid * y_grid]
    )


def banded(taps, rows, cols):
    offset = lax.broadcasted_iota(jnp.int32, (rows, cols), 1) - lax.broadcasted_iota(jnp.int32, (rows, cols), 0)
    picks = (offset[None] == jnp.arange(taps.shape[1])[:, None, None]).astype(jnp.float32)
    return jnp.einsum("ka,arc->krc", taps, picks, precision=lax.Precision.HIGHEST)


def separable(blocks, row_taps, col_taps, tile_rows, span):
    reach = row_taps.shape[1]
    down = banded(row_taps, tile_rows, tile_rows + reach - 1)
    across = jnp.swapaxes(banded(col_taps, span, span + reach - 1), 1, 2)
    passed = jnp.einsum("bac,kcd->bkad", blocks, across, precision=lax.Precision.HIGH)
    return jnp.einsum("kra,bkad->bkrd", down, passed, precision=lax.Precision.HIGH)


def local(template, row_taps, col_taps, coeffs, visits, boxes):
    half = row_taps.shape[1] // 2
    tile_rows, columns = template.shape
    tiles = lax.axis_size("tile")
    halves = lax.axis_size("zhi")
    group = lax.axis_size("xc")
    tile = lax.axis_index("tile")
    side = lax.axis_index("zhi")
    place = lax.axis_index("xc")
    full_width = columns * halves * group
    total_rows = tile_rows * tiles

    copies = jnp.broadcast_to(coeffs, (group,) + coeffs.shape[1:])
    half_coeffs = lax.all_to_all(copies, "xc", 0, 0, tiled=True)

    swap = [(h, halves - 1 - h) for h in range(halves)]
    pair = jnp.stack([template, lax.ppermute(template, "zhi", swap)])
    down = [(i, i + 1) for i in range(tiles - 1)]
    up = [(i + 1, i) for i in range(tiles - 1)]
    above = lax.ppermute(pair[:, tile_rows - half :], "tile", down)
    below = lax.ppermute(pair[:, :half], "tile", up)
    extended = jnp.concatenate([above, pair, below], axis=1)
    own = extended[0]
    other = extended[1]
    first = side == 0
    blocks = jnp.stack([jnp.where(first, own, other), jnp.where(first, other, own)])
    blocks = jnp.pad(blocks, ((0, 0), (0, 0), (2 * half, 2 * half)))
    span = columns + 2 * half
    y_coord = coordinate(tile * tile_rows, tile_rows, total_rows)
    basis = separable(blocks, row_taps, col_taps, tile_rows, span)
    models = []
    y = y_coord[:, None]
    for b in range(halves):
        start = (b * group + place) * columns - half
        x = coordinate(start, span, full_width)[None, :]
        w = jnp.einsum("vkt,krc->tvrc", half_coeffs, basis[b], precision=lax.Precision.HIGH)
        models.append(w[0] + x * w[1] + y * w[2] + (x * x) * w[3] + (x * y) * w[4] + (y * y) * w[5])
    models = jnp.stack(models, axis=1)
    parts = lax.all_to_all(models, "xc", 0, 0, tiled=True)
    parts = jnp.swapaxes(parts, 0, 1).reshape((halves * group,) + parts.shape[2:])
    core = parts[:, :, half : half + columns]
    left = parts[:, :, :half]
    right = parts[:, :, half + columns :]
    edge = jnp.zeros_like(left[:1])
    core = core.at[:, :, :half].add(jnp.concatenate([edge, right[:-1]], axis=0))
    core = core.at[:, :, columns - half :].add(jnp.concatenate([left[1:], edge], axis=0))
    model = jnp.swapaxes(core, 0, 1).reshape(1, tile_rows, full_width)

    visit = side * group + place
    local_boxes = lax.dynamic_slice_in_dim(boxes, visit, 1, 0)
    column_index = jnp.arange(full_width)
    inside = (column_index[None, :] >= local_boxes[:, 0:1]) & (
        column_index[None, :] < local_boxes[:, 0:1] + local_boxes[:, 1:2]
    )
    return jnp.where(inside[:, None, :], visits - model, jnp.float32(0.0))


def solution(mesh):
    tiles, visits = mesh.devices.shape
    split = Mesh(mesh.devices.reshape(tiles, 2, visits // 2), ("tile", "zhi", "xc"))
    cols = ("zhi", "xc")
    placed = (P("tile", cols), P(), P(), P(cols, None, None), P(cols, "tile", None), P())
    return jax.shard_map(
        local, mesh=split, in_specs=placed, out_specs=P(cols, "tile", None), check_vma=False
    )
```

```python
import jax
import jax.numpy as jnp
from jax import lax
from jax.sharding import Mesh
from jax.sharding import PartitionSpec as P


def coordinate(first, count, total):
    return 2.0 * ((first + jnp.arange(count)).astype(jnp.float32) + 0.5) / total - 1.0


def surface_terms(y_coord, x_coord):
    y_grid = y_coord[:, None] * jnp.ones_like(x_coord)[None, :]
    x_grid = jnp.ones_like(y_coord)[:, None] * x_coord[None, :]
    return jnp.stack(
        [jnp.ones_like(x_grid), x_grid, y_grid, x_grid * x_grid, x_grid * y_grid, y_grid * y_grid]
    )


def banded(taps, rows, cols):
    offset = lax.broadcasted_iota(jnp.int32, (rows, cols), 1) - lax.broadcasted_iota(jnp.int32, (rows, cols), 0)
    picks = (offset[None] == jnp.arange(taps.shape[1])[:, None, None]).astype(jnp.float32)
    return jnp.einsum("ka,arc->krc", taps, picks, precision=lax.Precision.HIGHEST)


def separable(blocks, row_taps, col_taps, tile_rows, span):
    reach = row_taps.shape[1]
    down = banded(row_taps, tile_rows, tile_rows + reach - 1)
    across = jnp.swapaxes(banded(col_taps, span, span + reach - 1), 1, 2)
    passed = jnp.einsum("bac,kcd->bkad", blocks, across, precision=lax.Precision.HIGH)
    return jnp.einsum("kra,bkad->bkrd", down, passed, precision=lax.Precision.HIGH)


def local(template, row_taps, col_taps, coeffs, visits, boxes):
    half = row_taps.shape[1] // 2
    tile_rows, columns = template.shape
    tiles = lax.axis_size("tile")
    halves = lax.axis_size("zhi")
    group = lax.axis_size("xc")
    tile = lax.axis_index("tile")
    side = lax.axis_index("zhi")
    place = lax.axis_index("xc")
    full_width = columns * halves * group
    total_rows = tile_rows * tiles


    swap = [(h, halves - 1 - h) for h in range(halves)]
    pair = jnp.stack([template, lax.ppermute(template, "zhi", swap)])
    down = [(i, i + 1) for i in range(tiles - 1)]
    up = [(i + 1, i) for i in range(tiles - 1)]
    above = lax.ppermute(pair[:, tile_rows - half :], "tile", down)
    below = lax.ppermute(pair[:, :half], "tile", up)
    copies = jnp.broadcast_to(coeffs, (group,) + coeffs.shape[1:])
    copies, pair = lax.optimization_barrier((copies, pair))
    half_coeffs = lax.all_to_all(copies, "xc", 0, 0, tiled=True)
    extended = jnp.concatenate([above, pair, below], axis=1)
    own = extended[0]
    other = extended[1]
    first = side == 0
    blocks = jnp.stack([jnp.where(first, own, other), jnp.where(first, other, own)])
    blocks = jnp.pad(blocks, ((0, 0), (0, 0), (2 * half, 2 * half)))
    span = columns + 2 * half
    y_coord = coordinate(tile * tile_rows, tile_rows, total_rows)
    basis = separable(blocks, row_taps, col_taps, tile_rows, span)
    models = []
    y = y_coord[:, None]
    for b in range(halves):
        start = (b * group + place) * columns - half
        x = coordinate(start, span, full_width)[None, :]
        w = jnp.einsum("vkt,krc->tvrc", half_coeffs, basis[b], precision=lax.Precision.HIGH)
        models.append(w[0] + x * w[1] + y * w[2] + (x * x) * w[3] + (x * y) * w[4] + (y * y) * w[5])
    models = jnp.stack(models, axis=1)
    parts = lax.all_to_all(models, "xc", 0, 0, tiled=True)
    parts = jnp.swapaxes(parts, 0, 1).reshape((halves * group,) + parts.shape[2:])
    core = parts[:, :, half : half + columns]
    left = parts[:, :, :half]
    right = parts[:, :, half + columns :]
    edge = jnp.zeros_like(left[:1])
    core = core.at[:, :, :half].add(jnp.concatenate([edge, right[:-1]], axis=0))
    core = core.at[:, :, columns - half :].add(jnp.concatenate([left[1:], edge], axis=0))
    model = jnp.swapaxes(core, 0, 1).reshape(1, tile_rows, full_width)

    visit = side * group + place
    local_boxes = lax.dynamic_slice_in_dim(boxes, visit, 1, 0)
    column_index = jnp.arange(full_width)
    inside = (column_index[None, :] >= local_boxes[:, 0:1]) & (
        column_index[None, :] < local_boxes[:, 0:1] + local_boxes[:, 1:2]
    )
    return jnp.where(inside[:, None, :], visits - model, jnp.float32(0.0))


def solution(mesh):
    tiles, visits = mesh.devices.shape
    split = Mesh(mesh.devices.reshape(tiles, 2, visits // 2), ("tile", "zhi", "xc"))
    cols = ("zhi", "xc")
    placed = (P("tile", cols), P(), P(), P(cols, None, None), P(cols, "tile", None), P())
    return jax.shard_map(
        local, mesh=split, in_specs=placed, out_specs=P(cols, "tile", None), check_vma=False
    )
```

```python
import jax
import jax.numpy as jnp
from jax import lax
from jax.sharding import Mesh
from jax.sharding import PartitionSpec as P


def coordinate(first, count, total):
    return 2.0 * ((first + jnp.arange(count)).astype(jnp.float32) + 0.5) / total - 1.0


def surface_terms(y_coord, x_coord):
    y_grid = y_coord[:, None] * jnp.ones_like(x_coord)[None, :]
    x_grid = jnp.ones_like(y_coord)[:, None] * x_coord[None, :]
    return jnp.stack(
        [jnp.ones_like(x_grid), x_grid, y_grid, x_grid * x_grid, x_grid * y_grid, y_grid * y_grid]
    )


def banded(taps, rows, cols):
    offset = lax.broadcasted_iota(jnp.int32, (rows, cols), 1) - lax.broadcasted_iota(jnp.int32, (rows, cols), 0)
    picks = (offset[None] == jnp.arange(taps.shape[1])[:, None, None]).astype(jnp.float32)
    return jnp.einsum("ka,arc->krc", taps, picks, precision=lax.Precision.HIGHEST)


def separable(blocks, row_taps, col_taps, tile_rows, span):
    reach = row_taps.shape[1]
    down = banded(row_taps, tile_rows, tile_rows + reach - 1)
    across = jnp.swapaxes(banded(col_taps, span, span + reach - 1), 1, 2)
    passed = jnp.einsum("bac,kcd->bkad", blocks, across, precision=lax.Precision.HIGH)
    return jnp.einsum("kra,bkad->bkrd", down, passed, precision=lax.Precision.HIGH)


def local(template, row_taps, col_taps, coeffs, visits, boxes):
    half = row_taps.shape[1] // 2
    tile_rows, columns = template.shape
    tiles = lax.axis_size("tile")
    halves = lax.axis_size("zhi")
    group = lax.axis_size("xc")
    tile = lax.axis_index("tile")
    side = lax.axis_index("zhi")
    place = lax.axis_index("xc")
    full_width = columns * halves * group
    total_rows = tile_rows * tiles


    swap = [(h, halves - 1 - h) for h in range(halves)]
    pair = jnp.stack([template, lax.ppermute(template, "zhi", swap)])
    down = [(i, i + 1) for i in range(tiles - 1)]
    up = [(i + 1, i) for i in range(tiles - 1)]
    above = lax.ppermute(pair[:, tile_rows - half :], "tile", down)
    below = lax.ppermute(pair[:, :half], "tile", up)
    copies = jnp.broadcast_to(coeffs, (group,) + coeffs.shape[1:])
    copies, pair = lax.optimization_barrier((copies, pair))
    half_coeffs = lax.all_to_all(copies, "xc", 0, 0, tiled=True)
    extended = jnp.concatenate([above, pair, below], axis=1)
    own = extended[0]
    other = extended[1]
    first = side == 0
    blocks = jnp.stack([jnp.where(first, own, other), jnp.where(first, other, own)])
    blocks = jnp.pad(blocks, ((0, 0), (0, 0), (2 * half, 2 * half)))
    span = columns + 2 * half
    y_coord = coordinate(tile * tile_rows, tile_rows, total_rows)
    basis = separable(blocks, row_taps, col_taps, tile_rows, span)
    models = []
    y = y_coord[:, None]
    for b in range(halves):
        start = (b * group + place) * columns - half
        x = coordinate(start, span, full_width)[None, :]
        w = jnp.einsum("vkt,krc->tvrc", half_coeffs, basis[b], precision=lax.Precision.HIGH)
        models.append(w[0] + x * w[1] + y * w[2] + (x * x) * w[3] + (x * y) * w[4] + (y * y) * w[5])
    models = jnp.stack(models, axis=1)
    parts = lax.all_to_all(models, "xc", 0, 0, tiled=True)
    parts = jnp.swapaxes(parts, 0, 1).reshape((halves * group,) + parts.shape[2:])
    core = parts[:, :, half : half + columns]
    left = parts[:, :, :half]
    right = parts[:, :, half + columns :]
    edge = jnp.zeros_like(left[:1])
    spill = ((0, 0), (0, 0), (0, columns - half))
    core = core + jnp.pad(jnp.concatenate([edge, right[:-1]], axis=0), spill)
    spill = ((0, 0), (0, 0), (columns - half, 0))
    core = core + jnp.pad(jnp.concatenate([left[1:], edge], axis=0), spill)
    model = jnp.swapaxes(core, 0, 1).reshape(1, tile_rows, full_width)

    visit = side * group + place
    local_boxes = lax.dynamic_slice_in_dim(boxes, visit, 1, 0)
    column_index = jnp.arange(full_width)
    inside = (column_index[None, :] >= local_boxes[:, 0:1]) & (
        column_index[None, :] < local_boxes[:, 0:1] + local_boxes[:, 1:2]
    )
    return jnp.where(inside[:, None, :], visits - model, jnp.float32(0.0))


def solution(mesh):
    tiles, visits = mesh.devices.shape
    split = Mesh(mesh.devices.reshape(tiles, 2, visits // 2), ("tile", "zhi", "xc"))
    cols = ("zhi", "xc")
    placed = (P("tile", cols), P(), P(), P(cols, None, None), P(cols, "tile", None), P())
    return jax.shard_map(
        local, mesh=split, in_specs=placed, out_specs=P(cols, "tile", None), check_vma=False
    )
```

```python
import jax
import jax.numpy as jnp
from jax import lax
from jax.sharding import Mesh
from jax.sharding import PartitionSpec as P


def coordinate(first, count, total):
    return 2.0 * ((first + jnp.arange(count)).astype(jnp.float32) + 0.5) / total - 1.0


def surface_terms(y_coord, x_coord):
    y_grid = y_coord[:, None] * jnp.ones_like(x_coord)[None, :]
    x_grid = jnp.ones_like(y_coord)[:, None] * x_coord[None, :]
    return jnp.stack(
        [jnp.ones_like(x_grid), x_grid, y_grid, x_grid * x_grid, x_grid * y_grid, y_grid * y_grid]
    )


def banded(taps, rows, cols):
    offset = lax.broadcasted_iota(jnp.int32, (rows, cols), 1) - lax.broadcasted_iota(jnp.int32, (rows, cols), 0)
    picks = (offset[None] == jnp.arange(taps.shape[1])[:, None, None]).astype(jnp.float32)
    return jnp.einsum("ka,arc->krc", taps, picks, precision=lax.Precision.HIGHEST)


def separable(blocks, row_taps, col_taps, tile_rows, span):
    reach = row_taps.shape[1]
    down = banded(row_taps, tile_rows, tile_rows + reach - 1)
    across = jnp.swapaxes(banded(col_taps, span, span + reach - 1), 1, 2)
    passed = jnp.einsum("bac,kcd->bkad", blocks, across, precision=lax.Precision.HIGHEST)
    return jnp.einsum("kra,bkad->bkrd", down, passed, precision=lax.Precision.HIGHEST)


def local(template, row_taps, col_taps, coeffs, visits, boxes):
    half = row_taps.shape[1] // 2
    tile_rows, columns = template.shape
    tiles = lax.axis_size("tile")
    halves = lax.axis_size("zhi")
    group = lax.axis_size("xc")
    tile = lax.axis_index("tile")
    side = lax.axis_index("zhi")
    place = lax.axis_index("xc")
    full_width = columns * halves * group
    total_rows = tile_rows * tiles


    swap = [(h, halves - 1 - h) for h in range(halves)]
    pair = jnp.stack([template, lax.ppermute(template, "zhi", swap)])
    down = [(i, i + 1) for i in range(tiles - 1)]
    up = [(i + 1, i) for i in range(tiles - 1)]
    above = lax.ppermute(pair[:, tile_rows - half :], "tile", down)
    below = lax.ppermute(pair[:, :half], "tile", up)
    copies = jnp.broadcast_to(coeffs, (group,) + coeffs.shape[1:])
    copies, pair = lax.optimization_barrier((copies, pair))
    half_coeffs = lax.all_to_all(copies, "xc", 0, 0, tiled=True)
    extended = jnp.concatenate([above, pair, below], axis=1)
    own = extended[0]
    other = extended[1]
    first = side == 0
    blocks = jnp.stack([jnp.where(first, own, other), jnp.where(first, other, own)])
    blocks = jnp.pad(blocks, ((0, 0), (0, 0), (2 * half, 2 * half)))
    span = columns + 2 * half
    y_coord = coordinate(tile * tile_rows, tile_rows, total_rows)
    basis = separable(blocks, row_taps, col_taps, tile_rows, span)
    models = []
    y = y_coord[:, None]
    for b in range(halves):
        start = (b * group + place) * columns - half
        x = coordinate(start, span, full_width)[None, :]
        w = jnp.einsum("vkt,krc->tvrc", half_coeffs, basis[b], precision=lax.Precision.HIGHEST)
        models.append(w[0] + x * w[1] + y * w[2] + (x * x) * w[3] + (x * y) * w[4] + (y * y) * w[5])
    models = jnp.stack(models, axis=1)
    parts = lax.all_to_all(models, "xc", 0, 0, tiled=True)
    parts = jnp.swapaxes(parts, 0, 1).reshape((halves * group,) + parts.shape[2:])
    core = parts[:, :, half : half + columns]
    left = parts[:, :, :half]
    right = parts[:, :, half + columns :]
    edge = jnp.zeros_like(left[:1])
    core = core.at[:, :, :half].add(jnp.concatenate([edge, right[:-1]], axis=0))
    core = core.at[:, :, columns - half :].add(jnp.concatenate([left[1:], edge], axis=0))
    model = jnp.swapaxes(core, 0, 1).reshape(1, tile_rows, full_width)

    visit = side * group + place
    local_boxes = lax.dynamic_slice_in_dim(boxes, visit, 1, 0)
    column_index = jnp.arange(full_width)
    inside = (column_index[None, :] >= local_boxes[:, 0:1]) & (
        column_index[None, :] < local_boxes[:, 0:1] + local_boxes[:, 1:2]
    )
    return jnp.where(inside[:, None, :], visits - model, jnp.float32(0.0))


def solution(mesh):
    tiles, visits = mesh.devices.shape
    split = Mesh(mesh.devices.reshape(tiles, 2, visits // 2), ("tile", "zhi", "xc"))
    cols = ("zhi", "xc")
    placed = (P("tile", cols), P(), P(), P(cols, None, None), P(cols, "tile", None), P())
    return jax.shard_map(
        local, mesh=split, in_specs=placed, out_specs=P(cols, "tile", None), check_vma=False
    )
```

```python
import jax
import jax.numpy as jnp
from jax import lax
from jax.sharding import Mesh
from jax.sharding import PartitionSpec as P


def coordinate(first, count, total):
    return 2.0 * ((first + jnp.arange(count)).astype(jnp.float32) + 0.5) / total - 1.0


def surface_terms(y_coord, x_coord):
    y_grid = y_coord[:, None] * jnp.ones_like(x_coord)[None, :]
    x_grid = jnp.ones_like(y_coord)[:, None] * x_coord[None, :]
    return jnp.stack(
        [jnp.ones_like(x_grid), x_grid, y_grid, x_grid * x_grid, x_grid * y_grid, y_grid * y_grid]
    )


def banded(taps, rows, cols):
    offset = lax.broadcasted_iota(jnp.int32, (rows, cols), 1) - lax.broadcasted_iota(jnp.int32, (rows, cols), 0)
    picks = (offset[None] == jnp.arange(taps.shape[1])[:, None, None]).astype(jnp.float32)
    return jnp.einsum("ka,arc->krc", taps, picks, precision=lax.Precision.HIGHEST)


def separable(blocks, row_taps, col_taps, tile_rows, span):
    reach = row_taps.shape[1]
    down = banded(row_taps, tile_rows, tile_rows + reach - 1)
    across = jnp.swapaxes(banded(col_taps, span, span + reach - 1), 1, 2)
    passed = jnp.einsum("bac,kcd->bkad", blocks, across, precision=lax.Precision.HIGH)
    return jnp.einsum("kra,bkad->bkrd", down, passed, precision=lax.Precision.HIGH)


def local(template, row_taps, col_taps, coeffs, visits, boxes):
    half = row_taps.shape[1] // 2
    tile_rows, columns = template.shape
    tiles = lax.axis_size("tile")
    halves = lax.axis_size("zhi")
    group = lax.axis_size("xc")
    tile = lax.axis_index("tile")
    side = lax.axis_index("zhi")
    place = lax.axis_index("xc")
    full_width = columns * halves * group
    total_rows = tile_rows * tiles


    down = [(i, i + 1) for i in range(tiles - 1)]
    up = [(i + 1, i) for i in range(tiles - 1)]
    above = lax.ppermute(template[tile_rows - half :], "tile", down)
    below = lax.ppermute(template[:half], "tile", up)
    own = jnp.concatenate([above, template, below], axis=0)
    swap = [(h, halves - 1 - h) for h in range(halves)]
    other = lax.ppermute(own, "zhi", swap)
    copies = jnp.broadcast_to(coeffs, (group,) + coeffs.shape[1:])
    copies, own = lax.optimization_barrier((copies, own))
    half_coeffs = lax.all_to_all(copies, "xc", 0, 0, tiled=True)
    first = side == 0
    blocks = jnp.stack([jnp.where(first, own, other), jnp.where(first, other, own)])
    blocks = jnp.pad(blocks, ((0, 0), (0, 0), (2 * half, 2 * half)))
    span = columns + 2 * half
    y_coord = coordinate(tile * tile_rows, tile_rows, total_rows)
    basis = separable(blocks, row_taps, col_taps, tile_rows, span)
    models = []
    y = y_coord[:, None]
    for b in range(halves):
        start = (b * group + place) * columns - half
        x = coordinate(start, span, full_width)[None, :]
        w = jnp.einsum("vkt,krc->tvrc", half_coeffs, basis[b], precision=lax.Precision.HIGH)
        models.append(w[0] + x * w[1] + y * w[2] + (x * x) * w[3] + (x * y) * w[4] + (y * y) * w[5])
    models = jnp.stack(models, axis=1)
    parts = lax.all_to_all(models, "xc", 0, 0, tiled=True)
    parts = jnp.swapaxes(parts, 0, 1).reshape((halves * group,) + parts.shape[2:])
    core = parts[:, :, half : half + columns]
    left = parts[:, :, :half]
    right = parts[:, :, half + columns :]
    edge = jnp.zeros_like(left[:1])
    core = core.at[:, :, :half].add(jnp.concatenate([edge, right[:-1]], axis=0))
    core = core.at[:, :, columns - half :].add(jnp.concatenate([left[1:], edge], axis=0))
    model = jnp.swapaxes(core, 0, 1).reshape(1, tile_rows, full_width)

    visit = side * group + place
    local_boxes = lax.dynamic_slice_in_dim(boxes, visit, 1, 0)
    column_index = jnp.arange(full_width)
    inside = (column_index[None, :] >= local_boxes[:, 0:1]) & (
        column_index[None, :] < local_boxes[:, 0:1] + local_boxes[:, 1:2]
    )
    return jnp.where(inside[:, None, :], visits - model, jnp.float32(0.0))


def solution(mesh):
    tiles, visits = mesh.devices.shape
    split = Mesh(mesh.devices.reshape(tiles, 2, visits // 2), ("tile", "zhi", "xc"))
    cols = ("zhi", "xc")
    placed = (P("tile", cols), P(), P(), P(cols, None, None), P(cols, "tile", None), P())
    return jax.shard_map(
        local, mesh=split, in_specs=placed, out_specs=P(cols, "tile", None), check_vma=False
    )
```

```python
import jax
import jax.numpy as jnp
from jax import lax
from jax.sharding import Mesh
from jax.sharding import PartitionSpec as P


def coordinate(first, count, total):
    return 2.0 * ((first + jnp.arange(count)).astype(jnp.float32) + 0.5) / total - 1.0


def surface_terms(y_coord, x_coord):
    y_grid = y_coord[:, None] * jnp.ones_like(x_coord)[None, :]
    x_grid = jnp.ones_like(y_coord)[:, None] * x_coord[None, :]
    return jnp.stack(
        [jnp.ones_like(x_grid), x_grid, y_grid, x_grid * x_grid, x_grid * y_grid, y_grid * y_grid]
    )


def banded(taps, rows, cols):
    offset = lax.broadcasted_iota(jnp.int32, (rows, cols), 1) - lax.broadcasted_iota(jnp.int32, (rows, cols), 0)
    picks = (offset[None] == jnp.arange(taps.shape[1])[:, None, None]).astype(jnp.float32)
    return jnp.einsum("ka,arc->krc", taps, picks, precision=lax.Precision.HIGH)


def separable(blocks, row_taps, col_taps, tile_rows, span):
    reach = row_taps.shape[1]
    down = banded(row_taps, tile_rows, tile_rows + reach - 1)
    across = jnp.swapaxes(banded(col_taps, span, span + reach - 1), 1, 2)
    passed = jnp.einsum("bac,kcd->bkad", blocks, across, precision=lax.Precision.HIGH)
    return jnp.einsum("kra,bkad->bkrd", down, passed, precision=lax.Precision.HIGH)


def local(template, row_taps, col_taps, coeffs, visits, boxes):
    half = row_taps.shape[1] // 2
    tile_rows, columns = template.shape
    tiles = lax.axis_size("tile")
    halves = lax.axis_size("zhi")
    group = lax.axis_size("xc")
    tile = lax.axis_index("tile")
    side = lax.axis_index("zhi")
    place = lax.axis_index("xc")
    full_width = columns * halves * group
    total_rows = tile_rows * tiles


    swap = [(h, halves - 1 - h) for h in range(halves)]
    pair = jnp.stack([template, lax.ppermute(template, "zhi", swap)])
    down = [(i, i + 1) for i in range(tiles - 1)]
    up = [(i + 1, i) for i in range(tiles - 1)]
    above = lax.ppermute(pair[:, tile_rows - half :], "tile", down)
    below = lax.ppermute(pair[:, :half], "tile", up)
    copies = jnp.broadcast_to(coeffs, (group,) + coeffs.shape[1:])
    copies, pair = lax.optimization_barrier((copies, pair))
    half_coeffs = lax.all_to_all(copies, "xc", 0, 0, tiled=True)
    extended = jnp.concatenate([above, pair, below], axis=1)
    own = extended[0]
    other = extended[1]
    first = side == 0
    blocks = jnp.stack([jnp.where(first, own, other), jnp.where(first, other, own)])
    blocks = jnp.pad(blocks, ((0, 0), (0, 0), (2 * half, 2 * half)))
    span = columns + 2 * half
    y_coord = coordinate(tile * tile_rows, tile_rows, total_rows)
    basis = separable(blocks, row_taps, col_taps, tile_rows, span)
    models = []
    y = y_coord[:, None]
    for b in range(halves):
        start = (b * group + place) * columns - half
        x = coordinate(start, span, full_width)[None, :]
        w = jnp.einsum("vkt,krc->tvrc", half_coeffs, basis[b], precision=lax.Precision.HIGH)
        models.append(w[0] + x * w[1] + y * w[2] + (x * x) * w[3] + (x * y) * w[4] + (y * y) * w[5])
    models = jnp.stack(models, axis=1)
    parts = lax.all_to_all(models, "xc", 0, 0, tiled=True)
    parts = jnp.swapaxes(parts, 0, 1).reshape((halves * group,) + parts.shape[2:])
    core = parts[:, :, half : half + columns]
    left = parts[:, :, :half]
    right = parts[:, :, half + columns :]
    edge = jnp.zeros_like(left[:1])
    core = core.at[:, :, :half].add(jnp.concatenate([edge, right[:-1]], axis=0))
    core = core.at[:, :, columns - half :].add(jnp.concatenate([left[1:], edge], axis=0))
    model = jnp.swapaxes(core, 0, 1).reshape(1, tile_rows, full_width)

    visit = side * group + place
    local_boxes = lax.dynamic_slice_in_dim(boxes, visit, 1, 0)
    column_index = jnp.arange(full_width)
    inside = (column_index[None, :] >= local_boxes[:, 0:1]) & (
        column_index[None, :] < local_boxes[:, 0:1] + local_boxes[:, 1:2]
    )
    return jnp.where(inside[:, None, :], visits - model, jnp.float32(0.0))


def solution(mesh):
    tiles, visits = mesh.devices.shape
    split = Mesh(mesh.devices.reshape(tiles, 2, visits // 2), ("tile", "zhi", "xc"))
    cols = ("zhi", "xc")
    placed = (P("tile", cols), P(), P(), P(cols, None, None), P(cols, "tile", None), P())
    return jax.shard_map(
        local, mesh=split, in_specs=placed, out_specs=P(cols, "tile", None), check_vma=False
    )
```

```python
import jax
import jax.numpy as jnp
from jax import lax
from jax.sharding import Mesh
from jax.sharding import PartitionSpec as P


def coordinate(first, count, total):
    return 2.0 * ((first + jnp.arange(count)).astype(jnp.float32) + 0.5) / total - 1.0


def surface_terms(y_coord, x_coord):
    y_grid = y_coord[:, None] * jnp.ones_like(x_coord)[None, :]
    x_grid = jnp.ones_like(y_coord)[:, None] * x_coord[None, :]
    return jnp.stack(
        [jnp.ones_like(x_grid), x_grid, y_grid, x_grid * x_grid, x_grid * y_grid, y_grid * y_grid]
    )


def banded(taps, rows, cols):
    offset = lax.broadcasted_iota(jnp.int32, (rows, cols), 1) - lax.broadcasted_iota(jnp.int32, (rows, cols), 0)
    picks = (offset[None] == jnp.arange(taps.shape[1])[:, None, None]).astype(jnp.float32)
    return jnp.einsum("ka,arc->krc", taps, picks, precision=lax.Precision.HIGH)


def separable(blocks, row_taps, col_taps, tile_rows, span):
    reach = row_taps.shape[1]
    down = banded(row_taps, tile_rows, tile_rows + reach - 1)
    across = jnp.swapaxes(banded(col_taps, span, span + reach - 1), 1, 2)
    passed = jnp.einsum("bac,kcd->bkad", blocks, across, precision=lax.Precision.HIGH)
    return jnp.einsum("kra,bkad->bkrd", down, passed, precision=lax.Precision.HIGH)


def local(template, row_taps, col_taps, coeffs, visits, boxes):
    half = row_taps.shape[1] // 2
    tile_rows, columns = template.shape
    tiles = lax.axis_size("tile")
    halves = lax.axis_size("zhi")
    group = lax.axis_size("xc")
    tile = lax.axis_index("tile")
    side = lax.axis_index("zhi")
    place = lax.axis_index("xc")
    full_width = columns * halves * group
    total_rows = tile_rows * tiles


    swap = [(h, halves - 1 - h) for h in range(halves)]
    pair = jnp.stack([template, lax.ppermute(template, "zhi", swap)])
    copies = jnp.broadcast_to(coeffs, (group,) + coeffs.shape[1:])
    copies, pair = lax.optimization_barrier((copies, pair))
    half_coeffs = lax.all_to_all(copies, "xc", 0, 0, tiled=True)
    half_coeffs, pair = lax.optimization_barrier((half_coeffs, pair))
    down = [(i, i + 1) for i in range(tiles - 1)]
    up = [(i + 1, i) for i in range(tiles - 1)]
    above = lax.ppermute(pair[:, tile_rows - half :], "tile", down)
    below = lax.ppermute(pair[:, :half], "tile", up)
    extended = jnp.concatenate([above, pair, below], axis=1)
    own = extended[0]
    other = extended[1]
    first = side == 0
    blocks = jnp.stack([jnp.where(first, own, other), jnp.where(first, other, own)])
    blocks = jnp.pad(blocks, ((0, 0), (0, 0), (2 * half, 2 * half)))
    span = columns + 2 * half
    y_coord = coordinate(tile * tile_rows, tile_rows, total_rows)
    basis = separable(blocks, row_taps, col_taps, tile_rows, span)
    models = []
    y = y_coord[:, None]
    for b in range(halves):
        start = (b * group + place) * columns - half
        x = coordinate(start, span, full_width)[None, :]
        w = jnp.einsum("vkt,krc->tvrc", half_coeffs, basis[b], precision=lax.Precision.HIGH)
        models.append(w[0] + x * w[1] + y * w[2] + (x * x) * w[3] + (x * y) * w[4] + (y * y) * w[5])
    models = jnp.stack(models, axis=1)
    parts = lax.all_to_all(models, "xc", 0, 0, tiled=True)
    parts = jnp.swapaxes(parts, 0, 1).reshape((halves * group,) + parts.shape[2:])
    core = parts[:, :, half : half + columns]
    left = parts[:, :, :half]
    right = parts[:, :, half + columns :]
    edge = jnp.zeros_like(left[:1])
    core = core.at[:, :, :half].add(jnp.concatenate([edge, right[:-1]], axis=0))
    core = core.at[:, :, columns - half :].add(jnp.concatenate([left[1:], edge], axis=0))
    model = jnp.swapaxes(core, 0, 1).reshape(1, tile_rows, full_width)

    visit = side * group + place
    local_boxes = lax.dynamic_slice_in_dim(boxes, visit, 1, 0)
    column_index = jnp.arange(full_width)
    inside = (column_index[None, :] >= local_boxes[:, 0:1]) & (
        column_index[None, :] < local_boxes[:, 0:1] + local_boxes[:, 1:2]
    )
    return jnp.where(inside[:, None, :], visits - model, jnp.float32(0.0))


def solution(mesh):
    tiles, visits = mesh.devices.shape
    split = Mesh(mesh.devices.reshape(tiles, 2, visits // 2), ("tile", "zhi", "xc"))
    cols = ("zhi", "xc")
    placed = (P("tile", cols), P(), P(), P(cols, None, None), P(cols, "tile", None), P())
    return jax.shard_map(
        local, mesh=split, in_specs=placed, out_specs=P(cols, "tile", None), check_vma=False
    )
```
